512 devices in a mesh: leaf: 128 (over x_lo, z, y), col: 4 (over x_hi, core).
Axes of the slice: x: 4 (x_hi: 2, x_lo: 2; x = x_hi * 2 + x_lo), y: 4, z: 16, core: 2. Of those that a mesh axis runs over, the one named last changes fastest.
Arguments:
- upper_block: bfloat16 [163840, 1024], P('leaf', 'col'), may hold values from -6 to 6
- lower_block: bfloat16 [131072, 1280], P(('leaf', 'col')), may hold values from -0.15625 to 0.15625
- pivot_inverse: bfloat16 [163840, 1280], P(('leaf', 'col')), may hold values from -1 to 2, as said below
- pivot_perm: int32 [128, 1280], P('leaf'), may hold values from 0 to 1279, each once within a row
- child_rhs: bfloat16 [163840, 128], P('leaf'), may hold values from -6 to 6
- pattern: int32 [128, 4], P('leaf'), may hold values from 0 to 63, as said below
- root_front: bfloat16 [16384, 16384], P(('leaf', 'col')), may hold values from -6 to 6
- root_rhs: bfloat16 [16384, 128], P(('leaf', 'col')), may hold values from -6 to 6
Outputs:
- assembled_front: bfloat16 [16384, 16384], P(('leaf', 'col'))
- assembled_rhs: float32 [16384, 128], P(('leaf', 'col'))
- child_forward: bfloat16 [163840, 128], P(('leaf', 'col'))
The draws below stay inside these ranges and needn't reach their ends.
Inputs may be any that keep to these rules, and one draw needn't show every extreme that they name: `pattern`: row k equals (k // 2) XOR s_a in column a, for 4 distinct values s_a shared by all rows; siblings 2 j and 2 j + 1 have equal rows. `pivot_inverse`: each block is an invertible matrix.
All inputs are finite; a program needn't handle non-finite values.
Results may differ from the reference program's by a relative error of at most 0.0047.
Values may be sent and summed in bfloat16 or wider, within the bound.
No kernel may reach another device: no remote copies, remote signals or barrier semaphores. Data moves between devices by JAX's collectives and lax.ppermute only.
A program may use at most 64 MiB of HBM per device.

```python
import math
import jax
import jax.numpy as jnp
from jax import lax

TILE = 256
PIV = 1280
RHS = 128
CHILDREN = 128
COUPLE = 4
CW = 1024
FRONT = 16384


def draw_pivot_inverse(key, part):
    noise = jax.random.truncated_normal(key, -4.0, 4.0, (CHILDREN, PIV, PIV), jnp.float32) * (0.6 / math.sqrt(PIV))
    matrices = noise + jnp.eye(PIV, dtype=jnp.float32)[None, :, :]
    return matrices.reshape(CHILDREN * PIV, PIV).astype(jnp.bfloat16)


def draw_pattern(key, part):
    half_count = CHILDREN // 2
    masks = jax.random.permutation(key, half_count)[:COUPLE].astype(jnp.int32)
    pairs = jnp.arange(CHILDREN, dtype=jnp.int32) // 2
    return jnp.bitwise_xor(pairs[:, None], masks[None, :]).astype(jnp.int32)


def level_of(own_key, dims, split, low, largest):
    level, own = 1.0, jax.random.fold_in(own_key, 6)
    for axis_at, blocks in split:
        steps = jnp.exp(jax.random.uniform(jax.random.fold_in(own, axis_at), (blocks,), jnp.float32, low / len(split), largest / len(split)))
        level = level * jnp.repeat(steps, dims[axis_at] // blocks).reshape([-1 if axis == axis_at else 1 for axis in range(len(dims))])
    return level


def scatter_about(key, dims, spread, limit, split=(), kind=jnp.bfloat16):
    array = spread * jax.random.normal(key, dims, jnp.float32)
    if split:
        array = array * level_of(key, dims, split, -0.22, 0.18)
    return jnp.clip(array, -limit, limit).astype(kind)


def setup_inputs(seed: int = 0) -> dict:
    key_list = jax.random.split(jax.random.key(seed), 9)
    return {
        "upper_block": scatter_about(key_list[0], (CHILDREN * PIV, CW), 1.0, 6.0, ((0, 128), (1, 4))),
        "lower_block": scatter_about(key_list[1], (CHILDREN * CW, PIV), PIV ** -0.5, 0.15625, ((0, 512),)),
        "pivot_inverse": draw_pivot_inverse(jax.random.fold_in(key_list[8], 71), 0),
        "pivot_perm": jax.vmap(lambda own: jax.random.permutation(own, PIV))(jax.random.split(key_list[3], CHILDREN)).reshape((CHILDREN, PIV)).astype(jnp.int32),
        "child_rhs": scatter_about(key_list[4], (CHILDREN * PIV, RHS), 1.0, 6.0, ((0, 128),)),
        "pattern": draw_pattern(jax.random.fold_in(key_list[8], 71), 0),
        "root_front": scatter_about(key_list[6], (FRONT, FRONT), 1.0, 6.0, ((0, 512),)),
        "root_rhs": scatter_about(key_list[7], (FRONT, RHS), 1.0, 6.0, ((0, 512),)),
    }


def eliminate_child(upper, lower, inverse, order, rhs):
    upper_rows = upper[order]
    rhs_rows = rhs[order]
    eliminated = jnp.dot(inverse, upper_rows, preferred_element_type=jnp.float32).astype(jnp.bfloat16)
    forward = jnp.dot(inverse, rhs_rows, preferred_element_type=jnp.float32).astype(jnp.bfloat16)
    update = -jnp.dot(lower, eliminated, preferred_element_type=jnp.float32)
    update_rhs = -jnp.dot(lower, forward, preferred_element_type=jnp.float32)
    return forward, update, update_rhs


def reference(upper_block, lower_block, pivot_inverse, pivot_perm, child_rhs, pattern, root_front, root_rhs):
    half_count = CHILDREN // 2
    uppers = upper_block.reshape(half_count, 2, PIV, CW)
    lowers = lower_block.reshape(half_count, 2, CW, PIV)
    inverses = pivot_inverse.reshape(half_count, 2, PIV, PIV)
    orders = pivot_perm.reshape(half_count, 2, PIV)
    rhs_blocks = child_rhs.reshape(half_count, 2, PIV, RHS)

    def per_pair(inputs):
        upper, lower, inverse, order, rhs = inputs
        first = eliminate_child(upper[0], lower[0], inverse[0], order[0], rhs[0])
        second = eliminate_child(upper[1], lower[1], inverse[1], order[1], rhs[1])
        forward = jnp.stack([first[0], second[0]])
        pair_update = (first[1] + second[1]).astype(jnp.bfloat16)
        pair_rhs = (first[2] + second[2]).astype(jnp.bfloat16)
        return forward, pair_update, pair_rhs

    forwards, pair_updates, pair_rhs = lax.map(per_pair, (uppers, lowers, inverses, orders, rhs_blocks))
    offsets = jnp.arange(TILE, dtype=jnp.int32)

    def extend_add(index, state):
        front_sum, rhs_sum = state
        tiles = lax.dynamic_index_in_dim(pattern, 2 * index, 0, keepdims=False).astype(jnp.int32)
        rows = (tiles[:, None] * TILE + offsets[None, :]).reshape(-1)
        update = lax.dynamic_index_in_dim(pair_updates, index, 0, keepdims=False).astype(jnp.float32)
        update_rhs = lax.dynamic_index_in_dim(pair_rhs, index, 0, keepdims=False).astype(jnp.float32)
        front_sum = front_sum.at[rows[:, None], rows[None, :]].add(update)
        rhs_sum = rhs_sum.at[rows].add(update_rhs)
        return front_sum, rhs_sum

    front_sum, rhs_sum = lax.fori_loop(0, half_count, extend_add, (root_front.astype(jnp.float32), root_rhs.astype(jnp.float32)))
    return front_sum.astype(jnp.bfloat16), rhs_sum, forwards.reshape(CHILDREN * PIV, RHS)
```

```python
import jax
import jax.numpy as jnp
from jax import lax
from jax.sharding import Mesh
from jax.sharding import PartitionSpec as P

LEAF = "leaf"
COLS = ("xh", "core")


def xor_route(value, mask_count):
    leaf_count = lax.axis_size(LEAF)

    def branch(mask):
        if mask == 0:
            return lambda x: x
        pairs = [(source, source ^ mask) for source in range(leaf_count)]
        return lambda x: lax.ppermute(x, LEAF, pairs)

    return [branch(2 * step) for step in range(mask_count)]


def body(
    upper_block, lower_block, pivot_inverse, pivot_perm, child_rhs, pattern, root_front, root_rhs
):
    leaf_count = lax.axis_size(LEAF)
    leaf_index = lax.axis_index(LEAF)
    piv = pivot_inverse.shape[1]
    share = pivot_inverse.shape[0]
    upper_x = lax.all_gather(upper_block, "xh", axis=0)
    upper_all = lax.all_gather(upper_x, "core", axis=0)
    order = pivot_perm[0]
    selector = (order[:, None] == lax.broadcasted_iota(jnp.int32, (piv, piv), 1)).astype(
        pivot_inverse.dtype
    )
    inverse_perm = jnp.dot(pivot_inverse, selector, preferred_element_type=jnp.float32).astype(
        pivot_inverse.dtype
    )
    forward = jnp.dot(inverse_perm, child_rhs, preferred_element_type=jnp.float32).astype(
        jnp.bfloat16
    )
    eliminated = jnp.einsum(
        "ip,cxpn->ixcn", inverse_perm, upper_all, preferred_element_type=jnp.float32
    ).astype(jnp.bfloat16)
    coupled_width = eliminated.shape[1] * eliminated.shape[2] * eliminated.shape[3]
    rows_out = jnp.concatenate([eliminated.reshape(share, coupled_width), forward], axis=1)
    rows_x = lax.all_gather(rows_out, "xh", axis=0)
    rows_all = lax.all_gather(rows_x, "core", axis=0)
    lower_rows = lower_block.shape[0]
    combined = -jnp.einsum(
        "rxcp,cxpn->rn",
        lower_block.reshape(lower_rows, 2, 2, share),
        rows_all,
        preferred_element_type=jnp.float32,
    )
    own_side = leaf_index % 2
    half_rows = lower_rows // 2
    own_rows = lax.dynamic_slice_in_dim(combined, own_side * half_rows, half_rows, 0)
    other_rows = lax.dynamic_slice_in_dim(combined, (1 - own_side) * half_rows, half_rows, 0)
    partner_rows = lax.ppermute(other_rows, LEAF, [(s, s ^ 1) for s in range(leaf_count)])
    moving = (own_rows + partner_rows).astype(jnp.bfloat16)
    col_count = 4
    share_rows = half_rows // col_count
    spread = lax.all_to_all(
        moving.reshape(col_count, share_rows, moving.shape[1]),
        COLS,
        split_axis=0,
        concat_axis=0,
        tiled=True,
    )
    column_masks = jnp.bitwise_xor(pattern[0], leaf_index // 2)
    branches = xor_route(None, leaf_count // 2)

    def route_piece(a, routed):
        piece = lax.dynamic_index_in_dim(spread, a, 0, keepdims=False)
        sent = lax.switch(column_masks[a], branches, piece)
        return lax.dynamic_update_index_in_dim(routed, sent, a, 0)

    routed = lax.fori_loop(0, col_count, route_piece, jnp.zeros_like(spread))
    tile_size = coupled_width // col_count
    front_part = routed[:, :, :coupled_width].reshape(col_count, share_rows, col_count, tile_size)
    tile_values = jnp.transpose(front_part, (1, 0, 2, 3)).reshape(
        share_rows, col_count * col_count, tile_size
    )
    target_tiles = jnp.bitwise_xor(
        jnp.bitwise_xor(column_masks[:, None], column_masks[None, :]), leaf_index // 2
    ).reshape(-1)
    front_width = root_front.shape[1]
    assembled = root_front.astype(jnp.float32).reshape(
        share_rows, front_width // tile_size, tile_size
    )
    assembled = assembled.at[:, target_tiles, :].add(tile_values.astype(jnp.float32))
    assembled_front = assembled.reshape(share_rows, front_width).astype(jnp.bfloat16)
    assembled_rhs = root_rhs.astype(jnp.float32) + jnp.sum(
        routed[:, :, coupled_width:].astype(jnp.float32), axis=0
    )
    return (assembled_front, assembled_rhs, forward)


def solution(mesh):
    leaf_count, col_count = mesh.devices.shape
    fine = Mesh(mesh.devices.reshape(leaf_count, 2, col_count // 2), (LEAF,) + COLS)
    rows = P((LEAF,) + COLS, None)
    return jax.shard_map(
        body,
        mesh=fine,
        in_specs=(
            P(LEAF, COLS),
            rows,
            rows,
            P(LEAF, None),
            P(LEAF, None),
            P(LEAF, None),
            rows,
            rows,
        ),
        out_specs=(rows, rows, rows),
        check_vma=False,
    )
```

```python
import jax
import jax.numpy as jnp
from jax import lax
from jax.sharding import Mesh
from jax.sharding import PartitionSpec as P

LEAF = "leaf"
COLS = ("xh", "core")


def xor_route(value, mask_count):
    leaf_count = lax.axis_size(LEAF)

    def branch(mask):
        if mask == 0:
            return lambda x: x
        pairs = [(source, source ^ mask) for source in range(leaf_count)]
        return lambda x: lax.ppermute(x, LEAF, pairs)

    return [branch(2 * step) for step in range(mask_count)]


def body(
    upper_block, lower_block, pivot_inverse, pivot_perm, child_rhs, pattern, root_front, root_rhs
):
    leaf_count = lax.axis_size(LEAF)
    leaf_index = lax.axis_index(LEAF)
    piv = pivot_inverse.shape[1]
    share = pivot_inverse.shape[0]
    upper_all = lax.all_gather(upper_block, COLS, axis=0)
    order = pivot_perm[0]
    selector = (order[:, None] == lax.broadcasted_iota(jnp.int32, (piv, piv), 1)).astype(
        pivot_inverse.dtype
    )
    inverse_perm = jnp.dot(pivot_inverse, selector, preferred_element_type=jnp.float32).astype(
        pivot_inverse.dtype
    )
    forward = jnp.dot(inverse_perm, child_rhs, preferred_element_type=jnp.float32).astype(
        jnp.bfloat16
    )
    eliminated = jnp.einsum(
        "ip,kpn->ikn", inverse_perm, upper_all, preferred_element_type=jnp.float32
    ).astype(jnp.bfloat16)
    coupled_width = eliminated.shape[1] * eliminated.shape[2]
    rows_out = jnp.concatenate([eliminated.reshape(share, coupled_width), forward], axis=1)
    rows_all = lax.all_gather(rows_out, COLS, axis=0)
    lower_rows = lower_block.shape[0]
    combined = -jnp.einsum(
        "rkp,kpn->rn",
        lower_block.reshape(lower_rows, 4, share),
        rows_all,
        preferred_element_type=jnp.float32,
    )
    own_side = leaf_index % 2
    half_rows = lower_rows // 2
    own_rows = lax.dynamic_slice_in_dim(combined, own_side * half_rows, half_rows, 0)
    other_rows = lax.dynamic_slice_in_dim(combined, (1 - own_side) * half_rows, half_rows, 0)
    partner_rows = lax.ppermute(other_rows, LEAF, [(s, s ^ 1) for s in range(leaf_count)])
    moving = (own_rows + partner_rows).astype(jnp.bfloat16)
    col_count = 4
    share_rows = half_rows // col_count
    spread = lax.all_to_all(
        moving.reshape(col_count, share_rows, moving.shape[1]),
        COLS,
        split_axis=0,
        concat_axis=0,
        tiled=True,
    )
    column_masks = jnp.bitwise_xor(pattern[0], leaf_index // 2)
    branches = xor_route(None, leaf_count // 2)

    def route_piece(a, routed):
        piece = lax.dynamic_index_in_dim(spread, a, 0, keepdims=False)
        sent = lax.switch(column_masks[a], branches, piece)
        return lax.dynamic_update_index_in_dim(routed, sent, a, 0)

    routed = lax.fori_loop(0, col_count, route_piece, jnp.zeros_like(spread))
    tile_size = coupled_width // col_count
    front_part = routed[:, :, :coupled_width].reshape(col_count, share_rows, col_count, tile_size)
    tile_values = jnp.transpose(front_part, (1, 0, 2, 3)).reshape(
        share_rows, col_count * col_count, tile_size
    )
    target_tiles = jnp.bitwise_xor(
        jnp.bitwise_xor(column_masks[:, None], column_masks[None, :]), leaf_index // 2
    ).reshape(-1)
    front_width = root_front.shape[1]
    assembled = root_front.astype(jnp.float32).reshape(
        share_rows, front_width // tile_size, tile_size
    )
    assembled = assembled.at[:, target_tiles, :].add(tile_values.astype(jnp.float32))
    assembled_front = assembled.reshape(share_rows, front_width).astype(jnp.bfloat16)
    assembled_rhs = root_rhs.astype(jnp.float32) + jnp.sum(
        routed[:, :, coupled_width:].astype(jnp.float32), axis=0
    )
    return (assembled_front, assembled_rhs, forward)


def solution(mesh):
    leaf_count, col_count = mesh.devices.shape
    fine = Mesh(mesh.devices.reshape(leaf_count, 2, col_count // 2), (LEAF,) + COLS)
    rows = P((LEAF,) + COLS, None)
    return jax.shard_map(
        body,
        mesh=fine,
        in_specs=(
            P(LEAF, COLS),
            rows,
            rows,
            P(LEAF, None),
            P(LEAF, None),
            P(LEAF, None),
            rows,
            rows,
        ),
        out_specs=(rows, rows, rows),
        check_vma=False,
    )
```

```python
import jax
import jax.numpy as jnp
from jax import lax
from jax.sharding import Mesh
from jax.sharding import PartitionSpec as P

LEAF = "leaf"
COLS = ("xh", "core")


def xor_route(value, mask_count):
    leaf_count = lax.axis_size(LEAF)

    def branch(mask):
        if mask == 0:
            return lambda x: x
        pairs = [(source, source ^ mask) for source in range(leaf_count)]
        return lambda x: lax.ppermute(x, LEAF, pairs)

    return [branch(2 * step) for step in range(mask_count)]


def col_gather(block):
    remote = lax.ppermute(block, COLS, [(c, c ^ 2) for c in range(4)])
    chip = jnp.stack([block, remote])
    partner = lax.ppermute(chip, COLS, [(c, c ^ 1) for c in range(4)])
    return jnp.concatenate([chip, partner])


def relative_order(col_index):
    flipped = jnp.bitwise_xor(jnp.arange(4, dtype=jnp.int32), col_index)
    return (flipped % 2) * 2 + flipped // 2


def body(
    upper_block, lower_block, pivot_inverse, pivot_perm, child_rhs, pattern, root_front, root_rhs
):
    leaf_count = lax.axis_size(LEAF)
    leaf_index = lax.axis_index(LEAF)
    piv = pivot_inverse.shape[1]
    share = pivot_inverse.shape[0]
    col_index = lax.axis_index(COLS)
    upper_all = col_gather(upper_block)
    order = pivot_perm[0]
    selector = (order[:, None] == lax.broadcasted_iota(jnp.int32, (piv, piv), 1)).astype(
        pivot_inverse.dtype
    )
    inverse_perm = jnp.dot(pivot_inverse, selector, preferred_element_type=jnp.float32).astype(
        pivot_inverse.dtype
    )
    forward = jnp.dot(inverse_perm, child_rhs, preferred_element_type=jnp.float32).astype(
        jnp.bfloat16
    )
    canonical = relative_order(col_index)
    eliminated = jnp.einsum(
        "ip,kpn->ikn", inverse_perm, jnp.take(upper_all, canonical, axis=0),
        preferred_element_type=jnp.float32,
    ).astype(jnp.bfloat16)
    coupled_width = eliminated.shape[1] * eliminated.shape[2]
    rows_out = jnp.concatenate([eliminated.reshape(share, coupled_width), forward], axis=1)
    rows_all = jnp.take(col_gather(rows_out), canonical, axis=0)
    lower_rows = lower_block.shape[0]
    combined = -jnp.einsum(
        "rkp,kpn->rn",
        lower_block.reshape(lower_rows, 4, share),
        rows_all,
        preferred_element_type=jnp.float32,
    )
    own_side = leaf_index % 2
    half_rows = lower_rows // 2
    own_rows = lax.dynamic_slice_in_dim(combined, own_side * half_rows, half_rows, 0)
    other_rows = lax.dynamic_slice_in_dim(combined, (1 - own_side) * half_rows, half_rows, 0)
    partner_rows = lax.ppermute(other_rows, LEAF, [(s, s ^ 1) for s in range(leaf_count)])
    moving = (own_rows + partner_rows).astype(jnp.bfloat16)
    col_count = 4
    share_rows = half_rows // col_count
    spread = lax.all_to_all(
        moving.reshape(col_count, share_rows, moving.shape[1]),
        COLS,
        split_axis=0,
        concat_axis=0,
        tiled=True,
    )
    column_masks = jnp.bitwise_xor(pattern[0], leaf_index // 2)
    branches = xor_route(None, leaf_count // 2)

    def route_piece(a, routed):
        piece = lax.dynamic_index_in_dim(spread, a, 0, keepdims=False)
        sent = lax.switch(column_masks[a], branches, piece)
        return lax.dynamic_update_index_in_dim(routed, sent, a, 0)

    routed = lax.fori_loop(0, col_count, route_piece, jnp.zeros_like(spread))
    tile_size = coupled_width // col_count
    front_part = routed[:, :, :coupled_width].reshape(col_count, share_rows, col_count, tile_size)
    tile_values = jnp.transpose(front_part, (1, 0, 2, 3)).reshape(
        share_rows, col_count * col_count, tile_size
    )
    target_tiles = jnp.bitwise_xor(
        jnp.bitwise_xor(column_masks[:, None], column_masks[None, :]), leaf_index // 2
    ).reshape(-1)
    front_width = root_front.shape[1]
    assembled = root_front.astype(jnp.float32).reshape(
        share_rows, front_width // tile_size, tile_size
    )
    assembled = assembled.at[:, target_tiles, :].add(tile_values.astype(jnp.float32))
    assembled_front = assembled.reshape(share_rows, front_width).astype(jnp.bfloat16)
    assembled_rhs = root_rhs.astype(jnp.float32) + jnp.sum(
        routed[:, :, coupled_width:].astype(jnp.float32), axis=0
    )
    return (assembled_front, assembled_rhs, forward)


def solution(mesh):
    leaf_count, col_count = mesh.devices.shape
    fine = Mesh(mesh.devices.reshape(leaf_count, 2, col_count // 2), (LEAF,) + COLS)
    rows = P((LEAF,) + COLS, None)
    return jax.shard_map(
        body,
        mesh=fine,
        in_specs=(
            P(LEAF, COLS),
            rows,
            rows,
            P(LEAF, None),
            P(LEAF, None),
            P(LEAF, None),
            rows,
            rows,
        ),
        out_specs=(rows, rows, rows),
        check_vma=False,
    )
```

```python
import jax
import jax.numpy as jnp
from jax import lax
from jax.sharding import Mesh
from jax.sharding import PartitionSpec as P

LEAF = "leaf"
COLS = ("xh", "core")


def xor_route(value, mask_count):
    leaf_count = lax.axis_size(LEAF)

    def branch(mask):
        if mask == 0:
            return lambda x: x
        pairs = [(source, source ^ mask) for source in range(leaf_count)]
        return lambda x: lax.ppermute(x, LEAF, pairs)

    return [branch(2 * step) for step in range(mask_count)]


def col_gather(block):
    remote = lax.ppermute(block, COLS, [(c, c ^ 2) for c in range(4)])
    chip = jnp.stack([block, remote])
    partner = lax.ppermute(chip, COLS, [(c, c ^ 1) for c in range(4)])
    return jnp.concatenate([chip, partner])


def relative_order(col_index):
    flipped = jnp.bitwise_xor(jnp.arange(4, dtype=jnp.int32), col_index)
    return (flipped % 2) * 2 + flipped // 2


def body(
    upper_block, lower_block, pivot_inverse, pivot_perm, child_rhs, pattern, root_front, root_rhs
):
    leaf_count = lax.axis_size(LEAF)
    leaf_index = lax.axis_index(LEAF)
    piv = pivot_inverse.shape[1]
    share = pivot_inverse.shape[0]
    col_index = lax.axis_index(COLS)
    upper_all = col_gather(upper_block)
    order = pivot_perm[0]
    selector = (order[:, None] == lax.broadcasted_iota(jnp.int32, (piv, piv), 1)).astype(
        pivot_inverse.dtype
    )
    inverse_perm = jnp.dot(pivot_inverse, selector, preferred_element_type=jnp.float32).astype(
        pivot_inverse.dtype
    )
    forward = jnp.dot(inverse_perm, child_rhs, preferred_element_type=jnp.float32).astype(
        jnp.bfloat16
    )
    canonical = relative_order(col_index)
    eliminated = jnp.take(
        jnp.einsum("ip,kpn->ikn", inverse_perm, upper_all, preferred_element_type=jnp.float32),
        canonical,
        axis=1,
    ).astype(jnp.bfloat16)
    coupled_width = eliminated.shape[1] * eliminated.shape[2]
    rows_out = jnp.concatenate([eliminated.reshape(share, coupled_width), forward], axis=1)
    rows_all = col_gather(rows_out)
    lower_rows = lower_block.shape[0]
    source_blocks = jnp.bitwise_xor(jnp.array([0, 2, 1, 3], jnp.int32), col_index)
    combined = -jnp.einsum(
        "rkp,kpn->rn",
        jnp.take(lower_block.reshape(lower_rows, 4, share), source_blocks, axis=1),
        rows_all,
        preferred_element_type=jnp.float32,
    )
    own_side = leaf_index % 2
    half_rows = lower_rows // 2
    own_rows = lax.dynamic_slice_in_dim(combined, own_side * half_rows, half_rows, 0)
    other_rows = lax.dynamic_slice_in_dim(combined, (1 - own_side) * half_rows, half_rows, 0)
    partner_rows = lax.ppermute(
        other_rows.astype(jnp.bfloat16), LEAF, [(s, s ^ 1) for s in range(leaf_count)]
    )
    moving = (own_rows + partner_rows.astype(jnp.float32)).astype(jnp.bfloat16)
    col_count = 4
    share_rows = half_rows // col_count
    spread = lax.all_to_all(
        moving.reshape(col_count, share_rows, moving.shape[1]),
        COLS,
        split_axis=0,
        concat_axis=0,
        tiled=True,
    )
    column_masks = jnp.bitwise_xor(pattern[0], leaf_index // 2)
    branches = xor_route(None, leaf_count // 2)

    def route_piece(a, routed):
        piece = lax.dynamic_index_in_dim(spread, a, 0, keepdims=False)
        sent = lax.switch(column_masks[a], branches, piece)
        return lax.dynamic_update_index_in_dim(routed, sent, a, 0)

    routed = lax.fori_loop(0, col_count, route_piece, jnp.zeros_like(spread))
    tile_size = coupled_width // col_count
    front_part = routed[:, :, :coupled_width].reshape(col_count, share_rows, col_count, tile_size)
    tile_values = jnp.transpose(front_part, (1, 0, 2, 3)).reshape(
        share_rows, col_count * col_count, tile_size
    )
    target_tiles = jnp.bitwise_xor(
        jnp.bitwise_xor(column_masks[:, None], column_masks[None, :]), leaf_index // 2
    ).reshape(-1)
    front_width = root_front.shape[1]
    assembled = root_front.astype(jnp.float32).reshape(
        share_rows, front_width // tile_size, tile_size
    )
    assembled = assembled.at[:, target_tiles, :].add(tile_values.astype(jnp.float32))
    assembled_front = assembled.reshape(share_rows, front_width).astype(jnp.bfloat16)
    assembled_rhs = root_rhs.astype(jnp.float32) + jnp.sum(
        routed[:, :, coupled_width:].astype(jnp.float32), axis=0
    )
    return (assembled_front, assembled_rhs, forward)


def solution(mesh):
    leaf_count, col_count = mesh.devices.shape
    fine = Mesh(mesh.devices.reshape(leaf_count, 2, col_count // 2), (LEAF,) + COLS)
    rows = P((LEAF,) + COLS, None)
    return jax.shard_map(
        body,
        mesh=fine,
        in_specs=(
            P(LEAF, COLS),
            rows,
            rows,
            P(LEAF, None),
            P(LEAF, None),
            P(LEAF, None),
            rows,
            rows,
        ),
        out_specs=(rows, rows, rows),
        check_vma=False,
    )
```

```python
import jax
import jax.numpy as jnp
from jax import lax
from jax.sharding import Mesh
from jax.sharding import PartitionSpec as P

LEAF = "leaf"
COLS = ("xh", "core")


def xor_route(value, mask_count):
    leaf_count = lax.axis_size(LEAF)

    def branch(mask):
        if mask == 0:
            return lambda x: x
        pairs = [(source, source ^ mask) for source in range(leaf_count)]
        return lambda x: lax.ppermute(x, LEAF, pairs)

    return [branch(2 * step) for step in range(mask_count)]


def col_gather(block):
    remote = lax.ppermute(block, COLS, [(c, c ^ 2) for c in range(4)])
    chip = jnp.stack([block, remote])
    partner = lax.ppermute(chip, COLS, [(c, c ^ 1) for c in range(4)])
    return jnp.concatenate([chip, partner])


def relative_order(col_index):
    flipped = jnp.bitwise_xor(jnp.arange(4, dtype=jnp.int32), col_index)
    return (flipped % 2) * 2 + flipped // 2


def body(
    upper_block, lower_block, pivot_inverse, pivot_perm, child_rhs, pattern, root_front, root_rhs
):
    leaf_count = lax.axis_size(LEAF)
    leaf_index = lax.axis_index(LEAF)
    piv = pivot_inverse.shape[1]
    share = pivot_inverse.shape[0]
    col_index = lax.axis_index(COLS)
    upper_all = col_gather(upper_block)
    order = pivot_perm[0]
    selector = (order[:, None] == lax.broadcasted_iota(jnp.int32, (piv, piv), 1)).astype(
        pivot_inverse.dtype
    )
    inverse_perm = jnp.dot(pivot_inverse, selector, preferred_element_type=jnp.float32).astype(
        pivot_inverse.dtype
    )
    forward = jnp.dot(inverse_perm, child_rhs, preferred_element_type=jnp.float32).astype(
        jnp.bfloat16
    )
    canonical = relative_order(col_index)
    eliminated = jnp.take(
        jnp.einsum("ip,kpn->ikn", inverse_perm, upper_all, preferred_element_type=jnp.float32),
        canonical,
        axis=1,
    ).astype(jnp.bfloat16)
    coupled_width = eliminated.shape[1] * eliminated.shape[2]
    rows_out = jnp.concatenate([eliminated.reshape(share, coupled_width), forward], axis=1)
    rows_all = col_gather(rows_out)
    lower_rows = lower_block.shape[0]
    source_blocks = jnp.bitwise_xor(jnp.array([0, 2, 1, 3], jnp.int32), col_index)
    combined = -jnp.einsum(
        "rkp,kpn->rn",
        jnp.take(lower_block.reshape(lower_rows, 4, share), source_blocks, axis=1),
        rows_all,
        preferred_element_type=jnp.float32,
    )
    own_side = leaf_index % 2
    half_rows = lower_rows // 2
    own_rows = lax.dynamic_slice_in_dim(combined, own_side * half_rows, half_rows, 0)
    other_rows = lax.dynamic_slice_in_dim(combined, (1 - own_side) * half_rows, half_rows, 0)
    partner_rows = lax.ppermute(
        other_rows.astype(jnp.bfloat16), LEAF, [(s, s ^ 1) for s in range(leaf_count)]
    )
    moving = (own_rows + partner_rows.astype(jnp.float32)).astype(jnp.bfloat16)
    col_count = 4
    share_rows = half_rows // col_count
    quarters = moving.reshape(col_count, share_rows, moving.shape[1])
    by_distance = [lax.dynamic_index_in_dim(quarters, col_index, 0, keepdims=False)]
    for distance in range(1, col_count):
        outgoing = lax.dynamic_index_in_dim(
            quarters, jnp.bitwise_xor(col_index, distance), 0, keepdims=False
        )
        by_distance.append(
            lax.ppermute(outgoing, COLS, [(c, c ^ distance) for c in range(col_count)])
        )
    spread = jnp.take(
        jnp.stack(by_distance),
        jnp.bitwise_xor(jnp.arange(col_count, dtype=jnp.int32), col_index),
        axis=0,
    )
    column_masks = jnp.bitwise_xor(pattern[0], leaf_index // 2)
    branches = xor_route(None, leaf_count // 2)

    def route_piece(a, routed):
        piece = lax.dynamic_index_in_dim(spread, a, 0, keepdims=False)
        sent = lax.switch(column_masks[a], branches, piece)
        return lax.dynamic_update_index_in_dim(routed, sent, a, 0)

    routed = lax.fori_loop(0, col_count, route_piece, jnp.zeros_like(spread))
    tile_size = coupled_width // col_count
    front_part = routed[:, :, :coupled_width].reshape(col_count, share_rows, col_count, tile_size)
    tile_values = jnp.transpose(front_part, (1, 0, 2, 3)).reshape(
        share_rows, col_count * col_count, tile_size
    )
    target_tiles = jnp.bitwise_xor(
        jnp.bitwise_xor(column_masks[:, None], column_masks[None, :]), leaf_index // 2
    ).reshape(-1)
    front_width = root_front.shape[1]
    assembled = root_front.astype(jnp.float32).reshape(
        share_rows, front_width // tile_size, tile_size
    )
    assembled = assembled.at[:, target_tiles, :].add(tile_values.astype(jnp.float32))
    assembled_front = assembled.reshape(share_rows, front_width).astype(jnp.bfloat16)
    assembled_rhs = root_rhs.astype(jnp.float32) + jnp.sum(
        routed[:, :, coupled_width:].astype(jnp.float32), axis=0
    )
    return (assembled_front, assembled_rhs, forward)


def solution(mesh):
    leaf_count, col_count = mesh.devices.shape
    fine = Mesh(mesh.devices.reshape(leaf_count, 2, col_count // 2), (LEAF,) + COLS)
    rows = P((LEAF,) + COLS, None)
    return jax.shard_map(
        body,
        mesh=fine,
        in_specs=(
            P(LEAF, COLS),
            rows,
            rows,
            P(LEAF, None),
            P(LEAF, None),
            P(LEAF, None),
            rows,
            rows,
        ),
        out_specs=(rows, rows, rows),
        check_vma=False,
    )
```

```python
import jax
import jax.numpy as jnp
from jax import lax
from jax.sharding import Mesh
from jax.sharding import PartitionSpec as P

LEAF = "leaf"
COLS = ("xh", "core")


def xor_route(value, mask_count):
    leaf_count = lax.axis_size(LEAF)

    def branch(mask):
        if mask == 0:
            return lambda x: x
        pairs = [(source, source ^ mask) for source in range(leaf_count)]
        return lambda x: lax.ppermute(x, LEAF, pairs)

    return [branch(2 * step) for step in range(mask_count)]


def col_gather(block):
    remote = lax.ppermute(block, COLS, [(c, c ^ 2) for c in range(4)])
    chip = jnp.stack([block, remote])
    partner = lax.ppermute(chip, COLS, [(c, c ^ 1) for c in range(4)])
    return jnp.concatenate([chip, partner])


def relative_order(col_index):
    flipped = jnp.bitwise_xor(jnp.arange(4, dtype=jnp.int32), col_index)
    return (flipped % 2) * 2 + flipped // 2


def body(
    upper_block, lower_block, pivot_inverse, pivot_perm, child_rhs, pattern, root_front, root_rhs
):
    leaf_count = lax.axis_size(LEAF)
    leaf_index = lax.axis_index(LEAF)
    piv = pivot_inverse.shape[1]
    share = pivot_inverse.shape[0]
    col_index = lax.axis_index(COLS)
    upper_all = col_gather(upper_block)
    order = pivot_perm[0]
    selector = (order[:, None] == lax.broadcasted_iota(jnp.int32, (piv, piv), 1)).astype(
        pivot_inverse.dtype
    )
    inverse_perm = jnp.dot(pivot_inverse, selector, preferred_element_type=jnp.float32).astype(
        pivot_inverse.dtype
    )
    forward = jnp.dot(inverse_perm, child_rhs, preferred_element_type=jnp.float32).astype(
        jnp.bfloat16
    )
    canonical = relative_order(col_index)
    eliminated = jnp.take(
        jnp.einsum("ip,kpn->ikn", inverse_perm, upper_all, preferred_element_type=jnp.float32),
        canonical,
        axis=1,
    ).astype(jnp.bfloat16)
    coupled_width = eliminated.shape[1] * eliminated.shape[2]
    rows_out = jnp.concatenate([eliminated.reshape(share, coupled_width), forward], axis=1)
    rows_all = col_gather(rows_out)
    lower_rows = lower_block.shape[0]
    source_blocks = jnp.bitwise_xor(jnp.array([0, 2, 1, 3], jnp.int32), col_index)
    combined = -jnp.einsum(
        "rkp,kpn->rn",
        jnp.take(lower_block.reshape(lower_rows, 4, share), source_blocks, axis=1),
        rows_all,
        preferred_element_type=jnp.float32,
    )
    own_side = leaf_index % 2
    half_rows = lower_rows // 2
    own_rows = lax.dynamic_slice_in_dim(combined, own_side * half_rows, half_rows, 0)
    other_rows = lax.dynamic_slice_in_dim(combined, (1 - own_side) * half_rows, half_rows, 0)
    partner_rows = lax.ppermute(
        other_rows.astype(jnp.bfloat16), LEAF, [(s, s ^ 1) for s in range(leaf_count)]
    )
    moving = (own_rows + partner_rows.astype(jnp.float32)).astype(jnp.bfloat16)
    col_count = 4
    share_rows = half_rows // col_count
    quarters = moving.reshape(col_count, share_rows, moving.shape[1])
    by_distance = [lax.dynamic_index_in_dim(quarters, col_index, 0, keepdims=False)]
    for distance in range(1, col_count):
        outgoing = lax.dynamic_index_in_dim(
            quarters, jnp.bitwise_xor(col_index, distance), 0, keepdims=False
        )
        by_distance.append(
            lax.ppermute(outgoing, COLS, [(c, c ^ distance) for c in range(col_count)])
        )
    spread = jnp.take(
        jnp.stack(by_distance),
        jnp.bitwise_xor(jnp.arange(col_count, dtype=jnp.int32), col_index),
        axis=0,
    )
    column_masks = jnp.bitwise_xor(pattern[0], leaf_index // 2)
    branches = xor_route(None, leaf_count // 2)

    def route_piece(a, routed):
        piece = lax.dynamic_index_in_dim(spread, a, 0, keepdims=False)
        sent = lax.switch(column_masks[a], branches, piece)
        return lax.dynamic_update_index_in_dim(routed, sent, a, 0)

    routed = lax.fori_loop(0, col_count, route_piece, jnp.zeros_like(spread))
    tile_size = coupled_width // col_count
    front_part = routed[:, :, :coupled_width].reshape(col_count, share_rows, col_count, tile_size)
    target_tiles = jnp.bitwise_xor(
        jnp.bitwise_xor(column_masks[:, None], column_masks[None, :]), leaf_index // 2
    )
    front_width = root_front.shape[1]
    placement = (
        target_tiles[:, :, None]
        == lax.broadcasted_iota(jnp.int32, (col_count, col_count, front_width // tile_size), 2)
    ).astype(front_part.dtype)
    by_row = jnp.transpose(front_part, (1, 0, 2, 3))
    update = lax.dot_general(
        jnp.broadcast_to(placement, (share_rows,) + placement.shape),
        by_row,
        (((1, 2), (1, 2)), ((0,), (0,))),
        preferred_element_type=jnp.float32,
    ).reshape(share_rows, front_width)
    assembled_front = (root_front.astype(jnp.float32) + update).astype(jnp.bfloat16)
    assembled_rhs = root_rhs.astype(jnp.float32) + jnp.sum(
        routed[:, :, coupled_width:].astype(jnp.float32), axis=0
    )
    return (assembled_front, assembled_rhs, forward)


def solution(mesh):
    leaf_count, col_count = mesh.devices.shape
    fine = Mesh(mesh.devices.reshape(leaf_count, 2, col_count // 2), (LEAF,) + COLS)
    rows = P((LEAF,) + COLS, None)
    return jax.shard_map(
        body,
        mesh=fine,
        in_specs=(
            P(LEAF, COLS),
            rows,
            rows,
            P(LEAF, None),
            P(LEAF, None),
            P(LEAF, None),
            rows,
            rows,
        ),
        out_specs=(rows, rows, rows),
        check_vma=False,
    )
```

```python
import jax
import jax.numpy as jnp
from jax import lax
from jax.sharding import Mesh
from jax.sharding import PartitionSpec as P

LEAF = "leaf"
COLS = ("xh", "core")


def xor_route(value, mask_count):
    leaf_count = lax.axis_size(LEAF)

    def branch(mask):
        if mask == 0:
            return lambda x: x
        pairs = [(source, source ^ mask) for source in range(leaf_count)]
        return lambda x: lax.ppermute(x, LEAF, pairs)

    return [branch(2 * step) for step in range(mask_count)]


def col_gather(block, beside=None):
    remote = lax.ppermute(block, COLS, [(c, c ^ 2) for c in range(4)])
    if beside is not None:
        remote, beside = lax.optimization_barrier((remote, beside))
    chip = jnp.stack([block, remote])
    partner = lax.ppermute(chip, COLS, [(c, c ^ 1) for c in range(4)])
    if beside is not None:
        return jnp.concatenate([chip, partner]), beside
    return jnp.concatenate([chip, partner])


def relative_order(col_index):
    flipped = jnp.bitwise_xor(jnp.arange(4, dtype=jnp.int32), col_index)
    return (flipped % 2) * 2 + flipped // 2


def body(
    upper_block, lower_block, pivot_inverse, pivot_perm, child_rhs, pattern, root_front, root_rhs
):
    leaf_count = lax.axis_size(LEAF)
    leaf_index = lax.axis_index(LEAF)
    piv = pivot_inverse.shape[1]
    share = pivot_inverse.shape[0]
    col_index = lax.axis_index(COLS)
    order = pivot_perm[0]
    selector = (order[:, None] == lax.broadcasted_iota(jnp.int32, (piv, piv), 1)).astype(
        pivot_inverse.dtype
    )
    inverse_perm = jnp.dot(pivot_inverse, selector, preferred_element_type=jnp.float32).astype(
        pivot_inverse.dtype
    )
    forward = jnp.dot(inverse_perm, child_rhs, preferred_element_type=jnp.float32).astype(
        jnp.bfloat16
    )
    upper_all, (inverse_perm, forward) = col_gather(upper_block, (inverse_perm, forward))
    canonical = relative_order(col_index)
    eliminated = jnp.take(
        jnp.einsum("ip,kpn->ikn", inverse_perm, upper_all, preferred_element_type=jnp.float32),
        canonical,
        axis=1,
    ).astype(jnp.bfloat16)
    coupled_width = eliminated.shape[1] * eliminated.shape[2]
    rows_out = jnp.concatenate([eliminated.reshape(share, coupled_width), forward], axis=1)
    rows_all = col_gather(rows_out)
    lower_rows = lower_block.shape[0]
    source_blocks = jnp.bitwise_xor(jnp.array([0, 2, 1, 3], jnp.int32), col_index)
    combined = -jnp.einsum(
        "rkp,kpn->rn",
        jnp.take(lower_block.reshape(lower_rows, 4, share), source_blocks, axis=1),
        rows_all,
        preferred_element_type=jnp.float32,
    )
    own_side = leaf_index % 2
    half_rows = lower_rows // 2
    own_rows = lax.dynamic_slice_in_dim(combined, own_side * half_rows, half_rows, 0)
    other_rows = lax.dynamic_slice_in_dim(combined, (1 - own_side) * half_rows, half_rows, 0)
    partner_rows = lax.ppermute(
        other_rows.astype(jnp.bfloat16), LEAF, [(s, s ^ 1) for s in range(leaf_count)]
    )
    moving = (own_rows + partner_rows.astype(jnp.float32)).astype(jnp.bfloat16)
    col_count = 4
    share_rows = half_rows // col_count
    quarters = moving.reshape(col_count, share_rows, moving.shape[1])
    by_distance = [lax.dynamic_index_in_dim(quarters, col_index, 0, keepdims=False)]
    for distance in range(1, col_count):
        outgoing = lax.dynamic_index_in_dim(
            quarters, jnp.bitwise_xor(col_index, distance), 0, keepdims=False
        )
        by_distance.append(
            lax.ppermute(outgoing, COLS, [(c, c ^ distance) for c in range(col_count)])
        )
    spread = jnp.take(
        jnp.stack(by_distance),
        jnp.bitwise_xor(jnp.arange(col_count, dtype=jnp.int32), col_index),
        axis=0,
    )
    column_masks = jnp.bitwise_xor(pattern[0], leaf_index // 2)
    branches = xor_route(None, leaf_count // 2)

    def route_piece(a, routed):
        piece = lax.dynamic_index_in_dim(spread, a, 0, keepdims=False)
        sent = lax.switch(column_masks[a], branches, piece)
        return lax.dynamic_update_index_in_dim(routed, sent, a, 0)

    routed = lax.fori_loop(0, col_count, route_piece, jnp.zeros_like(spread))
    tile_size = coupled_width // col_count
    front_part = routed[:, :, :coupled_width].reshape(col_count, share_rows, col_count, tile_size)
    target_tiles = jnp.bitwise_xor(
        jnp.bitwise_xor(column_masks[:, None], column_masks[None, :]), leaf_index // 2
    )
    front_width = root_front.shape[1]
    placement = (
        target_tiles[:, :, None]
        == lax.broadcasted_iota(jnp.int32, (col_count, col_count, front_width // tile_size), 2)
    ).astype(front_part.dtype)
    by_row = jnp.transpose(front_part, (1, 0, 2, 3))
    update = lax.dot_general(
        jnp.broadcast_to(placement, (share_rows,) + placement.shape),
        by_row,
        (((1, 2), (1, 2)), ((0,), (0,))),
        preferred_element_type=jnp.float32,
    ).reshape(share_rows, front_width)
    assembled_front = (root_front.astype(jnp.float32) + update).astype(jnp.bfloat16)
    assembled_rhs = root_rhs.astype(jnp.float32) + jnp.sum(
        routed[:, :, coupled_width:].astype(jnp.float32), axis=0
    )
    return (assembled_front, assembled_rhs, forward)


def solution(mesh):
    leaf_count, col_count = mesh.devices.shape
    fine = Mesh(mesh.devices.reshape(leaf_count, 2, col_count // 2), (LEAF,) + COLS)
    rows = P((LEAF,) + COLS, None)
    return jax.shard_map(
        body,
        mesh=fine,
        in_specs=(
            P(LEAF, COLS),
            rows,
            rows,
            P(LEAF, None),
            P(LEAF, None),
            P(LEAF, None),
            rows,
            rows,
        ),
        out_specs=(rows, rows, rows),
        check_vma=False,
    )
```

```python
import jax
import jax.numpy as jnp
from jax import lax
from jax.sharding import Mesh
from jax.sharding import PartitionSpec as P

LEAF = "leaf"
COLS = ("xh", "core")


def xor_route(value, mask_count):
    leaf_count = lax.axis_size(LEAF)

    def branch(mask):
        if mask == 0:
            return lambda x: x
        pairs = [(source, source ^ mask) for source in range(leaf_count)]
        return lambda x: lax.ppermute(x, LEAF, pairs)

    return [branch(2 * step) for step in range(mask_count)]


def col_gather(block):
    remote = lax.ppermute(block, COLS, [(c, c ^ 2) for c in range(4)])
    chip = jnp.stack([block, remote])
    partner = lax.ppermute(chip, COLS, [(c, c ^ 1) for c in range(4)])
    return jnp.concatenate([chip, partner])


def relative_order(col_index):
    flipped = jnp.bitwise_xor(jnp.arange(4, dtype=jnp.int32), col_index)
    return (flipped % 2) * 2 + flipped // 2


def body(
    upper_block, lower_block, pivot_inverse, pivot_perm, child_rhs, pattern, root_front, root_rhs
):
    leaf_count = lax.axis_size(LEAF)
    leaf_index = lax.axis_index(LEAF)
    piv = pivot_inverse.shape[1]
    share = pivot_inverse.shape[0]
    col_index = lax.axis_index(COLS)
    upper_all = col_gather(upper_block)
    order = pivot_perm[0]
    selector = (order[:, None] == lax.broadcasted_iota(jnp.int32, (piv, piv), 1)).astype(
        pivot_inverse.dtype
    )
    inverse_perm = jnp.dot(pivot_inverse, selector, preferred_element_type=jnp.float32).astype(
        pivot_inverse.dtype
    )
    forward = jnp.dot(inverse_perm, child_rhs, preferred_element_type=jnp.float32).astype(
        jnp.bfloat16
    )
    canonical = relative_order(col_index)
    eliminated = jnp.take(
        jnp.einsum("ip,kpn->ikn", inverse_perm, upper_all, preferred_element_type=jnp.float32),
        canonical,
        axis=1,
    ).astype(jnp.bfloat16)
    coupled_width = eliminated.shape[1] * eliminated.shape[2]
    rows_out = jnp.concatenate([eliminated.reshape(share, coupled_width), forward], axis=1)
    rows_all = col_gather(rows_out)
    lower_rows = lower_block.shape[0]
    source_blocks = jnp.bitwise_xor(jnp.array([0, 2, 1, 3], jnp.int32), col_index)
    combined = -jnp.einsum(
        "rkp,kpn->rn",
        jnp.take(lower_block.reshape(lower_rows, 4, share), source_blocks, axis=1),
        rows_all,
        preferred_element_type=jnp.float32,
    )
    own_side = leaf_index % 2
    half_rows = lower_rows // 2
    own_rows = lax.dynamic_slice_in_dim(combined, own_side * half_rows, half_rows, 0)
    other_rows = lax.dynamic_slice_in_dim(combined, (1 - own_side) * half_rows, half_rows, 0)
    col_count = 4
    share_rows = half_rows // col_count
    width = combined.shape[1]
    device_count = leaf_count * col_count
    everyone = (LEAF,) + COLS
    own_quarters = own_rows.reshape(col_count, share_rows, width)
    other_quarters = other_rows.astype(jnp.bfloat16).reshape(col_count, share_rows, width)
    by_distance = []
    for distance in range(col_count):
        target_quarter = jnp.bitwise_xor(col_index, distance)
        sibling_mask = col_count + distance
        from_sibling = lax.ppermute(
            lax.dynamic_index_in_dim(other_quarters, target_quarter, 0, keepdims=False),
            everyone,
            [(d, d ^ sibling_mask) for d in range(device_count)],
        )
        own = lax.dynamic_index_in_dim(own_quarters, target_quarter, 0, keepdims=False)
        if distance:
            own = lax.ppermute(own, everyone, [(d, d ^ distance) for d in range(device_count)])
        by_distance.append((own + from_sibling.astype(jnp.float32)).astype(jnp.bfloat16))
    spread = jnp.take(
        jnp.stack(by_distance),
        jnp.bitwise_xor(jnp.arange(col_count, dtype=jnp.int32), col_index),
        axis=0,
    )
    column_masks = jnp.bitwise_xor(pattern[0], leaf_index // 2)
    branches = xor_route(None, leaf_count // 2)

    def route_piece(a, routed):
        piece = lax.dynamic_index_in_dim(spread, a, 0, keepdims=False)
        sent = lax.switch(column_masks[a], branches, piece)
        return lax.dynamic_update_index_in_dim(routed, sent, a, 0)

    routed = lax.fori_loop(0, col_count, route_piece, jnp.zeros_like(spread))
    tile_size = coupled_width // col_count
    front_part = routed[:, :, :coupled_width].reshape(col_count, share_rows, col_count, tile_size)
    target_tiles = jnp.bitwise_xor(
        jnp.bitwise_xor(column_masks[:, None], column_masks[None, :]), leaf_index // 2
    )
    front_width = root_front.shape[1]
    placement = (
        target_tiles[:, :, None]
        == lax.broadcasted_iota(jnp.int32, (col_count, col_count, front_width // tile_size), 2)
    ).astype(front_part.dtype)
    by_row = jnp.transpose(front_part, (1, 0, 2, 3))
    update = lax.dot_general(
        jnp.broadcast_to(placement, (share_rows,) + placement.shape),
        by_row,
        (((1, 2), (1, 2)), ((0,), (0,))),
        preferred_element_type=jnp.float32,
    ).reshape(share_rows, front_width)
    assembled_front = (root_front.astype(jnp.float32) + update).astype(jnp.bfloat16)
    assembled_rhs = root_rhs.astype(jnp.float32) + jnp.sum(
        routed[:, :, coupled_width:].astype(jnp.float32), axis=0
    )
    return (assembled_front, assembled_rhs, forward)


def solution(mesh):
    leaf_count, col_count = mesh.devices.shape
    fine = Mesh(mesh.devices.reshape(leaf_count, 2, col_count // 2), (LEAF,) + COLS)
    rows = P((LEAF,) + COLS, None)
    return jax.shard_map(
        body,
        mesh=fine,
        in_specs=(
            P(LEAF, COLS),
            rows,
            rows,
            P(LEAF, None),
            P(LEAF, None),
            P(LEAF, None),
            rows,
            rows,
        ),
        out_specs=(rows, rows, rows),
        check_vma=False,
    )
```

```python
import jax
import jax.numpy as jnp
from jax import lax
from jax.sharding import Mesh
from jax.sharding import PartitionSpec as P

LEAF = "leaf"
COLS = ("xh", "core")


def xor_route(value, mask_count):
    leaf_count = lax.axis_size(LEAF)

    def branch(mask):
        if mask == 0:
            return lambda x: x
        pairs = [(source, source ^ mask) for source in range(leaf_count)]
        return lambda x: lax.ppermute(x, LEAF, pairs)

    return [branch(2 * step) for step in range(mask_count)]


def col_gather(block):
    remote = lax.ppermute(block, COLS, [(c, c ^ 2) for c in range(4)])
    chip = jnp.stack([block, remote])
    partner = lax.ppermute(chip, COLS, [(c, c ^ 1) for c in range(4)])
    return jnp.concatenate([chip, partner])


def relative_order(col_index):
    flipped = jnp.bitwise_xor(jnp.arange(4, dtype=jnp.int32), col_index)
    return (flipped % 2) * 2 + flipped // 2


def body(
    upper_block, lower_block, pivot_inverse, pivot_perm, child_rhs, pattern, root_front, root_rhs
):
    leaf_count = lax.axis_size(LEAF)
    leaf_index = lax.axis_index(LEAF)
    piv = pivot_inverse.shape[1]
    share = pivot_inverse.shape[0]
    col_index = lax.axis_index(COLS)
    upper_all = col_gather(upper_block)
    order = pivot_perm[0]
    selector = (order[:, None] == lax.broadcasted_iota(jnp.int32, (piv, piv), 1)).astype(
        pivot_inverse.dtype
    )
    inverse_perm = jnp.dot(pivot_inverse, selector, preferred_element_type=jnp.float32).astype(
        pivot_inverse.dtype
    )
    forward = jnp.dot(inverse_perm, child_rhs, preferred_element_type=jnp.float32).astype(
        jnp.bfloat16
    )
    canonical = relative_order(col_index)
    eliminated = jnp.take(
        jnp.einsum("ip,kpn->ikn", inverse_perm, upper_all, preferred_element_type=jnp.float32),
        canonical,
        axis=1,
    ).astype(jnp.bfloat16)
    coupled_width = eliminated.shape[1] * eliminated.shape[2]
    rows_out = jnp.concatenate([eliminated.reshape(share, coupled_width), forward], axis=1)
    rows_all = col_gather(rows_out)
    lower_rows = lower_block.shape[0]
    source_blocks = jnp.bitwise_xor(jnp.array([0, 2, 1, 3], jnp.int32), col_index)
    combined = -jnp.einsum(
        "rkp,kpn->rn",
        jnp.take(lower_block.reshape(lower_rows, 4, share), source_blocks, axis=1),
        rows_all,
        preferred_element_type=jnp.float32,
    )
    own_side = leaf_index % 2
    half_rows = lower_rows // 2
    own_rows = lax.dynamic_slice_in_dim(combined, own_side * half_rows, half_rows, 0)
    other_rows = lax.dynamic_slice_in_dim(combined, (1 - own_side) * half_rows, half_rows, 0)
    partner_rows = lax.ppermute(
        other_rows.astype(jnp.bfloat16), LEAF, [(s, s ^ 1) for s in range(leaf_count)]
    )
    moving = (own_rows + partner_rows.astype(jnp.float32)).astype(jnp.bfloat16)
    col_count = 4
    share_rows = half_rows // col_count
    spread = lax.all_to_all(
        moving.reshape(col_count, share_rows, moving.shape[1]),
        COLS,
        split_axis=0,
        concat_axis=0,
        tiled=True,
    )
    column_masks = jnp.bitwise_xor(pattern[0], leaf_index // 2)
    branches = xor_route(None, leaf_count // 2)

    def route_piece(a, routed):
        piece = lax.dynamic_index_in_dim(spread, a, 0, keepdims=False)
        sent = lax.switch(column_masks[a], branches, piece)
        return lax.dynamic_update_index_in_dim(routed, sent, a, 0)

    routed = lax.fori_loop(0, col_count, route_piece, jnp.zeros_like(spread))
    tile_size = coupled_width // col_count
    front_part = routed[:, :, :coupled_width].reshape(col_count, share_rows, col_count, tile_size)
    target_tiles = jnp.bitwise_xor(
        jnp.bitwise_xor(column_masks[:, None], column_masks[None, :]), leaf_index // 2
    )
    front_width = root_front.shape[1]
    placement = (
        target_tiles[:, :, None]
        == lax.broadcasted_iota(jnp.int32, (col_count, col_count, front_width // tile_size), 2)
    ).astype(front_part.dtype)
    by_row = jnp.transpose(front_part, (1, 0, 2, 3))
    update = lax.dot_general(
        jnp.broadcast_to(placement, (share_rows,) + placement.shape),
        by_row,
        (((1, 2), (1, 2)), ((0,), (0,))),
        preferred_element_type=jnp.float32,
    ).reshape(share_rows, front_width)
    assembled_front = (root_front.astype(jnp.float32) + update).astype(jnp.bfloat16)
    assembled_rhs = root_rhs.astype(jnp.float32) + jnp.sum(
        routed[:, :, coupled_width:].astype(jnp.float32), axis=0
    )
    return (assembled_front, assembled_rhs, forward)


def solution(mesh):
    leaf_count, col_count = mesh.devices.shape
    fine = Mesh(mesh.devices.reshape(leaf_count, 2, col_count // 2), (LEAF,) + COLS)
    rows = P((LEAF,) + COLS, None)
    return jax.shard_map(
        body,
        mesh=fine,
        in_specs=(
            P(LEAF, COLS),
            rows,
            rows,
            P(LEAF, None),
            P(LEAF, None),
            P(LEAF, None),
            rows,
            rows,
        ),
        out_specs=(rows, rows, rows),
        check_vma=False,
    )
```

```python
import jax
import jax.numpy as jnp
from jax import lax
from jax.sharding import Mesh
from jax.sharding import PartitionSpec as P

LEAF = "leaf"
COLS = ("xh", "core")


def xor_route(value, mask_count):
    leaf_count = lax.axis_size(LEAF)

    def branch(mask):
        if mask == 0:
            return lambda x: x
        pairs = [(source, source ^ mask) for source in range(leaf_count)]
        return lambda x: lax.ppermute(x, LEAF, pairs)

    return [branch(2 * step) for step in range(mask_count)]


def col_gather(block):
    remote = lax.ppermute(block, COLS, [(c, c ^ 2) for c in range(4)])
    chip = jnp.stack([block, remote])
    partner = lax.ppermute(chip, COLS, [(c, c ^ 1) for c in range(4)])
    return chip, partner


def relative_order(col_index):
    flipped = jnp.bitwise_xor(jnp.arange(4, dtype=jnp.int32), col_index)
    return (flipped % 2) * 2 + flipped // 2


def body(
    upper_block, lower_block, pivot_inverse, pivot_perm, child_rhs, pattern, root_front, root_rhs
):
    leaf_count = lax.axis_size(LEAF)
    leaf_index = lax.axis_index(LEAF)
    piv = pivot_inverse.shape[1]
    share = pivot_inverse.shape[0]
    col_index = lax.axis_index(COLS)
    upper_all = col_gather(upper_block)
    order = pivot_perm[0]
    selector = (order[:, None] == lax.broadcasted_iota(jnp.int32, (piv, piv), 1)).astype(
        pivot_inverse.dtype
    )
    inverse_perm = jnp.dot(pivot_inverse, selector, preferred_element_type=jnp.float32).astype(
        pivot_inverse.dtype
    )
    forward = jnp.dot(inverse_perm, child_rhs, preferred_element_type=jnp.float32).astype(
        jnp.bfloat16
    )
    canonical = relative_order(col_index)
    eliminated = jnp.take(
        jnp.einsum(
            "ip,kpn->ikn",
            inverse_perm,
            jnp.concatenate(upper_all),
            preferred_element_type=jnp.float32,
        ),
        canonical,
        axis=1,
    ).astype(jnp.bfloat16)
    coupled_width = eliminated.shape[1] * eliminated.shape[2]
    rows_out = jnp.concatenate([eliminated.reshape(share, coupled_width), forward], axis=1)
    rows_all = col_gather(rows_out)
    lower_rows = lower_block.shape[0]
    source_blocks = jnp.bitwise_xor(jnp.array([0, 2, 1, 3], jnp.int32), col_index)
    lower_parts = jnp.take(lower_block.reshape(lower_rows, 4, share), source_blocks, axis=1)
    chip_rows, partner_rows = rows_all
    chip_part = jnp.einsum(
        "rkp,kpn->rn", lower_parts[:, :2], chip_rows, preferred_element_type=jnp.float32
    )
    chip_part, partner_rows = lax.optimization_barrier((chip_part, partner_rows))
    combined = -(
        chip_part
        + jnp.einsum(
            "rkp,kpn->rn", lower_parts[:, 2:], partner_rows, preferred_element_type=jnp.float32
        )
    )
    own_side = leaf_index % 2
    half_rows = lower_rows // 2
    own_rows = lax.dynamic_slice_in_dim(combined, own_side * half_rows, half_rows, 0)
    other_rows = lax.dynamic_slice_in_dim(combined, (1 - own_side) * half_rows, half_rows, 0)
    partner_rows = lax.ppermute(
        other_rows.astype(jnp.bfloat16), LEAF, [(s, s ^ 1) for s in range(leaf_count)]
    )
    moving = (own_rows + partner_rows.astype(jnp.float32)).astype(jnp.bfloat16)
    col_count = 4
    share_rows = half_rows // col_count
    quarters = moving.reshape(col_count, share_rows, moving.shape[1])
    by_distance = [lax.dynamic_index_in_dim(quarters, col_index, 0, keepdims=False)]
    for distance in range(1, col_count):
        outgoing = lax.dynamic_index_in_dim(
            quarters, jnp.bitwise_xor(col_index, distance), 0, keepdims=False
        )
        by_distance.append(
            lax.ppermute(outgoing, COLS, [(c, c ^ distance) for c in range(col_count)])
        )
    spread = jnp.take(
        jnp.stack(by_distance),
        jnp.bitwise_xor(jnp.arange(col_count, dtype=jnp.int32), col_index),
        axis=0,
    )
    column_masks = jnp.bitwise_xor(pattern[0], leaf_index // 2)
    branches = xor_route(None, leaf_count // 2)

    def route_piece(a, routed):
        piece = lax.dynamic_index_in_dim(spread, a, 0, keepdims=False)
        sent = lax.switch(column_masks[a], branches, piece)
        return lax.dynamic_update_index_in_dim(routed, sent, a, 0)

    routed = lax.fori_loop(0, col_count, route_piece, jnp.zeros_like(spread))
    tile_size = coupled_width // col_count
    front_part = routed[:, :, :coupled_width].reshape(col_count, share_rows, col_count, tile_size)
    target_tiles = jnp.bitwise_xor(
        jnp.bitwise_xor(column_masks[:, None], column_masks[None, :]), leaf_index // 2
    )
    front_width = root_front.shape[1]
    placement = (
        target_tiles[:, :, None]
        == lax.broadcasted_iota(jnp.int32, (col_count, col_count, front_width // tile_size), 2)
    ).astype(front_part.dtype)
    by_row = jnp.transpose(front_part, (1, 0, 2, 3))
    update = lax.dot_general(
        jnp.broadcast_to(placement, (share_rows,) + placement.shape),
        by_row,
        (((1, 2), (1, 2)), ((0,), (0,))),
        preferred_element_type=jnp.float32,
    ).reshape(share_rows, front_width)
    assembled_front = (root_front.astype(jnp.float32) + update).astype(jnp.bfloat16)
    assembled_rhs = root_rhs.astype(jnp.float32) + jnp.sum(
        routed[:, :, coupled_width:].astype(jnp.float32), axis=0
    )
    return (assembled_front, assembled_rhs, forward)


def solution(mesh):
    leaf_count, col_count = mesh.devices.shape
    fine = Mesh(mesh.devices.reshape(leaf_count, 2, col_count // 2), (LEAF,) + COLS)
    rows = P((LEAF,) + COLS, None)
    return jax.shard_map(
        body,
        mesh=fine,
        in_specs=(
            P(LEAF, COLS),
            rows,
            rows,
            P(LEAF, None),
            P(LEAF, None),
            P(LEAF, None),
            rows,
            rows,
        ),
        out_specs=(rows, rows, rows),
        check_vma=False,
    )
```

```python
import jax
import jax.numpy as jnp
from jax import lax
from jax.sharding import Mesh
from jax.sharding import PartitionSpec as P

LEAF = "leaf"
COLS = ("xh", "core")


def xor_route(value, mask_count):
    leaf_count = lax.axis_size(LEAF)

    def branch(mask):
        if mask == 0:
            return lambda x: x
        pairs = [(source, source ^ mask) for source in range(leaf_count)]
        return lambda x: lax.ppermute(x, LEAF, pairs)

    return [branch(2 * step) for step in range(mask_count)]


def col_gather(block):
    remote = lax.ppermute(block, COLS, [(c, c ^ 2) for c in range(4)])
    chip = jnp.stack([block, remote])
    partner = lax.ppermute(chip, COLS, [(c, c ^ 1) for c in range(4)])
    return chip, partner


def relative_order(col_index):
    flipped = jnp.bitwise_xor(jnp.arange(4, dtype=jnp.int32), col_index)
    return (flipped % 2) * 2 + flipped // 2


def body(
    upper_block, lower_block, pivot_inverse, pivot_perm, child_rhs, pattern, root_front, root_rhs
):
    leaf_count = lax.axis_size(LEAF)
    leaf_index = lax.axis_index(LEAF)
    piv = pivot_inverse.shape[1]
    share = pivot_inverse.shape[0]
    col_index = lax.axis_index(COLS)
    upper_all = col_gather(upper_block)
    order = pivot_perm[0]
    selector = (order[:, None] == lax.broadcasted_iota(jnp.int32, (piv, piv), 1)).astype(
        pivot_inverse.dtype
    )
    inverse_perm = jnp.dot(pivot_inverse, selector, preferred_element_type=jnp.float32).astype(
        pivot_inverse.dtype
    )
    forward = jnp.dot(inverse_perm, child_rhs, preferred_element_type=jnp.float32).astype(
        jnp.bfloat16
    )
    canonical = relative_order(col_index)
    eliminated = jnp.take(
        jnp.einsum(
            "ip,kpn->ikn",
            inverse_perm,
            jnp.concatenate(upper_all),
            preferred_element_type=jnp.float32,
        ),
        canonical,
        axis=1,
    ).astype(jnp.bfloat16)
    coupled_width = eliminated.shape[1] * eliminated.shape[2]
    rows_out = jnp.concatenate([eliminated.reshape(share, coupled_width), forward], axis=1)
    lower_rows = lower_block.shape[0]
    source_blocks = jnp.bitwise_xor(jnp.array([0, 2, 1, 3], jnp.int32), col_index)
    lower_parts = jnp.take(lower_block.reshape(lower_rows, 4, share), source_blocks, axis=1)
    rows_remote = lax.ppermute(rows_out, COLS, [(c, c ^ 2) for c in range(4)])
    own_part = jnp.dot(lower_parts[:, 0], rows_out, preferred_element_type=jnp.float32)
    own_part, rows_remote = lax.optimization_barrier((own_part, rows_remote))
    partner_rows = lax.ppermute(
        jnp.stack([rows_out, rows_remote]), COLS, [(c, c ^ 1) for c in range(4)]
    )
    remote_part = jnp.dot(lower_parts[:, 1], rows_remote, preferred_element_type=jnp.float32)
    remote_part, partner_rows = lax.optimization_barrier((remote_part, partner_rows))
    combined = -(
        own_part
        + remote_part
        + jnp.einsum(
            "rkp,kpn->rn", lower_parts[:, 2:], partner_rows, preferred_element_type=jnp.float32
        )
    )
    own_side = leaf_index % 2
    half_rows = lower_rows // 2
    own_rows = lax.dynamic_slice_in_dim(combined, own_side * half_rows, half_rows, 0)
    other_rows = lax.dynamic_slice_in_dim(combined, (1 - own_side) * half_rows, half_rows, 0)
    partner_rows = lax.ppermute(
        other_rows.astype(jnp.bfloat16), LEAF, [(s, s ^ 1) for s in range(leaf_count)]
    )
    moving = (own_rows + partner_rows.astype(jnp.float32)).astype(jnp.bfloat16)
    col_count = 4
    share_rows = half_rows // col_count
    quarters = moving.reshape(col_count, share_rows, moving.shape[1])
    by_distance = [lax.dynamic_index_in_dim(quarters, col_index, 0, keepdims=False)]
    for distance in range(1, col_count):
        outgoing = lax.dynamic_index_in_dim(
            quarters, jnp.bitwise_xor(col_index, distance), 0, keepdims=False
        )
        by_distance.append(
            lax.ppermute(outgoing, COLS, [(c, c ^ distance) for c in range(col_count)])
        )
    spread = jnp.take(
        jnp.stack(by_distance),
        jnp.bitwise_xor(jnp.arange(col_count, dtype=jnp.int32), col_index),
        axis=0,
    )
    column_masks = jnp.bitwise_xor(pattern[0], leaf_index // 2)
    branches = xor_route(None, leaf_count // 2)

    def route_piece(a, routed):
        piece = lax.dynamic_index_in_dim(spread, a, 0, keepdims=False)
        sent = lax.switch(column_masks[a], branches, piece)
        return lax.dynamic_update_index_in_dim(routed, sent, a, 0)

    routed = lax.fori_loop(0, col_count, route_piece, jnp.zeros_like(spread))
    tile_size = coupled_width // col_count
    front_part = routed[:, :, :coupled_width].reshape(col_count, share_rows, col_count, tile_size)
    target_tiles = jnp.bitwise_xor(
        jnp.bitwise_xor(column_masks[:, None], column_masks[None, :]), leaf_index // 2
    )
    front_width = root_front.shape[1]
    placement = (
        target_tiles[:, :, None]
        == lax.broadcasted_iota(jnp.int32, (col_count, col_count, front_width // tile_size), 2)
    ).astype(front_part.dtype)
    by_row = jnp.transpose(front_part, (1, 0, 2, 3))
    update = lax.dot_general(
        jnp.broadcast_to(placement, (share_rows,) + placement.shape),
        by_row,
        (((1, 2), (1, 2)), ((0,), (0,))),
        preferred_element_type=jnp.float32,
    ).reshape(share_rows, front_width)
    assembled_front = (root_front.astype(jnp.float32) + update).astype(jnp.bfloat16)
    assembled_rhs = root_rhs.astype(jnp.float32) + jnp.sum(
        routed[:, :, coupled_width:].astype(jnp.float32), axis=0
    )
    return (assembled_front, assembled_rhs, forward)


def solution(mesh):
    leaf_count, col_count = mesh.devices.shape
    fine = Mesh(mesh.devices.reshape(leaf_count, 2, col_count // 2), (LEAF,) + COLS)
    rows = P((LEAF,) + COLS, None)
    return jax.shard_map(
        body,
        mesh=fine,
        in_specs=(
            P(LEAF, COLS),
            rows,
            rows,
            P(LEAF, None),
            P(LEAF, None),
            P(LEAF, None),
            rows,
            rows,
        ),
        out_specs=(rows, rows, rows),
        check_vma=False,
    )
```

```python
import jax
import jax.numpy as jnp
from jax import lax
from jax.sharding import Mesh
from jax.sharding import PartitionSpec as P

LEAF = "leaf"
COLS = ("xh", "core")


def xor_route(value, mask_count):
    leaf_count = lax.axis_size(LEAF)

    def branch(mask):
        if mask == 0:
            return lambda x: x
        pairs = [(source, source ^ mask) for source in range(leaf_count)]
        return lambda x: lax.ppermute(x, LEAF, pairs)

    return [branch(2 * step) for step in range(mask_count)]


def col_gather(block):
    remote = lax.ppermute(block, COLS, [(c, c ^ 2) for c in range(4)])
    chip = jnp.stack([block, remote])
    partner = lax.ppermute(chip, COLS, [(c, c ^ 1) for c in range(4)])
    return chip, partner


def relative_order(col_index):
    flipped = jnp.bitwise_xor(jnp.arange(4, dtype=jnp.int32), col_index)
    return (flipped % 2) * 2 + flipped // 2


def body(
    upper_block, lower_block, pivot_inverse, pivot_perm, child_rhs, pattern, root_front, root_rhs
):
    leaf_count = lax.axis_size(LEAF)
    leaf_index = lax.axis_index(LEAF)
    piv = pivot_inverse.shape[1]
    share = pivot_inverse.shape[0]
    col_index = lax.axis_index(COLS)
    upper_all = col_gather(upper_block)
    order = pivot_perm[0]
    selector = (order[:, None] == lax.broadcasted_iota(jnp.int32, (piv, piv), 1)).astype(
        pivot_inverse.dtype
    )
    inverse_perm = jnp.dot(pivot_inverse, selector, preferred_element_type=jnp.float32).astype(
        pivot_inverse.dtype
    )
    forward = jnp.dot(inverse_perm, child_rhs, preferred_element_type=jnp.float32).astype(
        jnp.bfloat16
    )
    canonical = relative_order(col_index)
    eliminated = jnp.take(
        jnp.einsum(
            "ip,kpn->ikn",
            inverse_perm,
            jnp.concatenate(upper_all),
            preferred_element_type=jnp.float32,
        ),
        canonical,
        axis=1,
    ).astype(jnp.bfloat16)
    coupled_width = eliminated.shape[1] * eliminated.shape[2]
    rows_out = jnp.concatenate([eliminated.reshape(share, coupled_width), forward], axis=1)
    rows_all = col_gather(rows_out)
    lower_rows = lower_block.shape[0]
    source_blocks = jnp.bitwise_xor(jnp.array([0, 2, 1, 3], jnp.int32), col_index)
    lower_parts = jnp.take(lower_block.reshape(lower_rows, 4, share), source_blocks, axis=1)
    chip_rows, partner_rows = rows_all
    chip_part = jnp.einsum(
        "rkp,kpn->rn", lower_parts[:, :2], chip_rows, preferred_element_type=jnp.float32
    )
    chip_part, partner_rows = lax.optimization_barrier((chip_part, partner_rows))
    combined = -(
        chip_part
        + jnp.einsum(
            "rkp,kpn->rn", lower_parts[:, 2:], partner_rows, preferred_element_type=jnp.float32
        )
    )
    own_side = leaf_index % 2
    half_rows = lower_rows // 2
    own_rows = lax.dynamic_slice_in_dim(combined, own_side * half_rows, half_rows, 0)
    other_rows = lax.dynamic_slice_in_dim(combined, (1 - own_side) * half_rows, half_rows, 0)
    partner_rows = lax.ppermute(
        other_rows.astype(jnp.bfloat16), LEAF, [(s, s ^ 1) for s in range(leaf_count)]
    )
    moving = (own_rows + partner_rows.astype(jnp.float32)).astype(jnp.bfloat16)
    col_count = 4
    share_rows = half_rows // col_count
    quarters = moving.reshape(col_count, share_rows, moving.shape[1])
    by_distance = [lax.dynamic_index_in_dim(quarters, col_index, 0, keepdims=False)]
    for distance in range(1, col_count):
        outgoing = lax.dynamic_index_in_dim(
            quarters, jnp.bitwise_xor(col_index, distance), 0, keepdims=False
        )
        by_distance.append(
            lax.ppermute(outgoing, COLS, [(c, c ^ distance) for c in range(col_count)])
        )
    spread = jnp.take(
        jnp.stack(by_distance),
        jnp.bitwise_xor(jnp.arange(col_count, dtype=jnp.int32), col_index),
        axis=0,
    )
    column_masks = jnp.bitwise_xor(pattern[0], leaf_index // 2)
    branches = xor_route(None, leaf_count // 2)

    def route_piece(a, routed):
        piece = lax.dynamic_index_in_dim(spread, a, 0, keepdims=False)
        sent = lax.switch(column_masks[a], branches, piece)
        return lax.dynamic_update_index_in_dim(routed, sent, a, 0)

    routed = lax.fori_loop(0, col_count, route_piece, spread)
    tile_size = coupled_width // col_count
    front_part = routed[:, :, :coupled_width].reshape(col_count, share_rows, col_count, tile_size)
    target_tiles = jnp.bitwise_xor(
        jnp.bitwise_xor(column_masks[:, None], column_masks[None, :]), leaf_index // 2
    )
    front_width = root_front.shape[1]
    placement = (
        target_tiles[:, :, None]
        == lax.broadcasted_iota(jnp.int32, (col_count, col_count, front_width // tile_size), 2)
    ).astype(front_part.dtype)
    by_row = jnp.transpose(front_part, (1, 0, 2, 3))
    update = lax.dot_general(
        jnp.broadcast_to(placement, (share_rows,) + placement.shape),
        by_row,
        (((1, 2), (1, 2)), ((0,), (0,))),
        preferred_element_type=jnp.float32,
    ).reshape(share_rows, front_width)
    assembled_front = (root_front.astype(jnp.float32) + update).astype(jnp.bfloat16)
    assembled_rhs = root_rhs.astype(jnp.float32) + jnp.sum(
        routed[:, :, coupled_width:].astype(jnp.float32), axis=0
    )
    return (assembled_front, assembled_rhs, forward)


def solution(mesh):
    leaf_count, col_count = mesh.devices.shape
    fine = Mesh(mesh.devices.reshape(leaf_count, 2, col_count // 2), (LEAF,) + COLS)
    rows = P((LEAF,) + COLS, None)
    return jax.shard_map(
        body,
        mesh=fine,
        in_specs=(
            P(LEAF, COLS),
            rows,
            rows,
            P(LEAF, None),
            P(LEAF, None),
            P(LEAF, None),
            rows,
            rows,
        ),
        out_specs=(rows, rows, rows),
        check_vma=False,
    )
```

```python
import jax
import jax.numpy as jnp
from jax import lax
from jax.sharding import Mesh
from jax.sharding import PartitionSpec as P

LEAF = "leaf"
COLS = ("xh", "core")


def xor_route(value, mask_count):
    leaf_count = lax.axis_size(LEAF)

    def branch(mask):
        if mask == 0:
            return lambda x: x
        pairs = [(source, source ^ mask) for source in range(leaf_count)]
        return lambda x: lax.ppermute(x, LEAF, pairs)

    return [branch(2 * step) for step in range(mask_count)]


def col_gather(block, beside=None):
    remote = lax.ppermute(block, COLS, [(c, c ^ 2) for c in range(4)])
    if beside is not None:
        remote, beside = lax.optimization_barrier((remote, beside))
    chip = jnp.stack([block, remote])
    partner = lax.ppermute(chip, COLS, [(c, c ^ 1) for c in range(4)])
    if beside is not None:
        return (chip, partner), beside
    return chip, partner


def relative_order(col_index):
    flipped = jnp.bitwise_xor(jnp.arange(4, dtype=jnp.int32), col_index)
    return (flipped % 2) * 2 + flipped // 2


def body(
    upper_block, lower_block, pivot_inverse, pivot_perm, child_rhs, pattern, root_front, root_rhs
):
    leaf_count = lax.axis_size(LEAF)
    leaf_index = lax.axis_index(LEAF)
    piv = pivot_inverse.shape[1]
    share = pivot_inverse.shape[0]
    col_index = lax.axis_index(COLS)
    lower_rows = lower_block.shape[0]
    source_blocks = jnp.bitwise_xor(jnp.array([0, 2, 1, 3], jnp.int32), col_index)
    lower_parts = jnp.take(lower_block.reshape(lower_rows, 4, share), source_blocks, axis=1)
    upper_all, lower_parts = col_gather(upper_block, lower_parts)
    order = pivot_perm[0]
    selector = (order[:, None] == lax.broadcasted_iota(jnp.int32, (piv, piv), 1)).astype(
        pivot_inverse.dtype
    )
    inverse_perm = jnp.dot(pivot_inverse, selector, preferred_element_type=jnp.float32).astype(
        pivot_inverse.dtype
    )
    forward = jnp.dot(inverse_perm, child_rhs, preferred_element_type=jnp.float32).astype(
        jnp.bfloat16
    )
    canonical = relative_order(col_index)
    eliminated = jnp.take(
        jnp.einsum(
            "ip,kpn->ikn",
            inverse_perm,
            jnp.concatenate(upper_all),
            preferred_element_type=jnp.float32,
        ),
        canonical,
        axis=1,
    ).astype(jnp.bfloat16)
    coupled_width = eliminated.shape[1] * eliminated.shape[2]
    rows_out = jnp.concatenate([eliminated.reshape(share, coupled_width), forward], axis=1)
    rows_all = col_gather(rows_out)
    chip_rows, partner_rows = rows_all
    chip_part = jnp.einsum(
        "rkp,kpn->rn", lower_parts[:, :2], chip_rows, preferred_element_type=jnp.float32
    )
    chip_part, partner_rows = lax.optimization_barrier((chip_part, partner_rows))
    combined = -(
        chip_part
        + jnp.einsum(
            "rkp,kpn->rn", lower_parts[:, 2:], partner_rows, preferred_element_type=jnp.float32
        )
    )
    own_side = leaf_index % 2
    half_rows = lower_rows // 2
    own_rows = lax.dynamic_slice_in_dim(combined, own_side * half_rows, half_rows, 0)
    other_rows = lax.dynamic_slice_in_dim(combined, (1 - own_side) * half_rows, half_rows, 0)
    partner_rows = lax.ppermute(
        other_rows.astype(jnp.bfloat16), LEAF, [(s, s ^ 1) for s in range(leaf_count)]
    )
    moving = (own_rows + partner_rows.astype(jnp.float32)).astype(jnp.bfloat16)
    col_count = 4
    share_rows = half_rows // col_count
    quarters = moving.reshape(col_count, share_rows, moving.shape[1])
    by_distance = [lax.dynamic_index_in_dim(quarters, col_index, 0, keepdims=False)]
    for distance in range(1, col_count):
        outgoing = lax.dynamic_index_in_dim(
            quarters, jnp.bitwise_xor(col_index, distance), 0, keepdims=False
        )
        by_distance.append(
            lax.ppermute(outgoing, COLS, [(c, c ^ distance) for c in range(col_count)])
        )
    spread = jnp.take(
        jnp.stack(by_distance),
        jnp.bitwise_xor(jnp.arange(col_count, dtype=jnp.int32), col_index),
        axis=0,
    )
    column_masks = jnp.bitwise_xor(pattern[0], leaf_index // 2)
    branches = xor_route(None, leaf_count // 2)

    def route_piece(a, routed):
        piece = lax.dynamic_index_in_dim(spread, a, 0, keepdims=False)
        sent = lax.switch(column_masks[a], branches, piece)
        return lax.dynamic_update_index_in_dim(routed, sent, a, 0)

    routed = lax.fori_loop(0, col_count, route_piece, spread)
    tile_size = coupled_width // col_count
    front_part = routed[:, :, :coupled_width].reshape(col_count, share_rows, col_count, tile_size)
    target_tiles = jnp.bitwise_xor(
        jnp.bitwise_xor(column_masks[:, None], column_masks[None, :]), leaf_index // 2
    )
    front_width = root_front.shape[1]
    placement = (
        target_tiles[:, :, None]
        == lax.broadcasted_iota(jnp.int32, (col_count, col_count, front_width // tile_size), 2)
    ).astype(front_part.dtype)
    by_row = jnp.transpose(front_part, (1, 0, 2, 3))
    update = lax.dot_general(
        jnp.broadcast_to(placement, (share_rows,) + placement.shape),
        by_row,
        (((1, 2), (1, 2)), ((0,), (0,))),
        preferred_element_type=jnp.float32,
    ).reshape(share_rows, front_width)
    assembled_front = (root_front.astype(jnp.float32) + update).astype(jnp.bfloat16)
    assembled_rhs = root_rhs.astype(jnp.float32) + jnp.sum(
        routed[:, :, coupled_width:].astype(jnp.float32), axis=0
    )
    return (assembled_front, assembled_rhs, forward)


def solution(mesh):
    leaf_count, col_count = mesh.devices.shape
    fine = Mesh(mesh.devices.reshape(leaf_count, 2, col_count // 2), (LEAF,) + COLS)
    rows = P((LEAF,) + COLS, None)
    return jax.shard_map(
        body,
        mesh=fine,
        in_specs=(
            P(LEAF, COLS),
            rows,
            rows,
            P(LEAF, None),
            P(LEAF, None),
            P(LEAF, None),
            rows,
            rows,
        ),
        out_specs=(rows, rows, rows),
        check_vma=False,
    )
```
